256 devices in a mesh: tm: 64 (over y, z, core), freq: 4 (over x).
Axes of the slice: x: 4, y: 4, z: 8, core: 2. Of those that a mesh axis runs over, the one named last changes fastest.
Arguments:
- visibility: float32 [64, 2, 4096, 1024], P('freq', None, 'tm'), may hold values from -6 to 6
- codebook: bfloat16 [16, 8, 64, 128], replicated, may hold values from -0.1875 to 0.1875
- block_index: int32 [64, 64, 16, 16], P('tm', 'freq'), may hold values from -1 to 7, as said below
- block_scale: float32 [64, 64, 16, 16], P('tm', 'freq'), may hold values from 0.5 to 2
- fg_basis: float32 [16, 64, 64], replicated, may hold values from -0.75 to 0.75
- fg_count: int32 [64], P('tm'), may hold values from 1 to 32
Outputs:
- filtered: float32 [64, 64, 16, 128], P('tm', 'freq')
The draws below stay inside these ranges and needn't reach their ends.
Inputs may be any that keep to these rules, and one draw needn't show every extreme that they name: `block_index`: -1 marks an absent block; block (k, f, j, l) is absent whenever 64 * l + 63 < 15 * k; other entries name a pattern.
All inputs are finite; a program needn't handle non-finite values.
Results may differ from the reference program's by a relative error of at most 0.014.
Values may be sent and summed in bfloat16 or wider, within the bound.
No kernel may reach another device: no remote copies, remote signals or barrier semaphores. Data moves between devices by JAX's collectives and lax.ppermute only.
A program may use at most 128 MiB of HBM per device.

```python
import math
import jax
import jax.numpy as jnp
from jax import lax

TIME_SAMPLES = 4096
BASELINE_COUNT = 1024
CHANNEL_COUNT = 64
BLOCK_WIDTH = 64
PATTERN_CODES = 8
MODES = 64
MSTEP = 15
MULTIPOLE_BLOCKS = 16
BBLOCKS = 16


def draw_block_index(key, part):
    code_draw = jax.random.randint(key, (MODES, CHANNEL_COUNT, BBLOCKS, MULTIPOLE_BLOCKS), 0, PATTERN_CODES, dtype=jnp.int32)
    mode_value = MSTEP * jnp.arange(MODES, dtype=jnp.int32)
    lblock_ids = jnp.arange(MULTIPOLE_BLOCKS, dtype=jnp.int32)
    bblock_ids = jnp.arange(BBLOCKS, dtype=jnp.int32)
    above_mode = lblock_ids[None, :] * BLOCK_WIDTH + BLOCK_WIDTH - 1 >= mode_value[:, None]
    in_reach = lblock_ids[None, :] <= MULTIPOLE_BLOCKS // 4 + bblock_ids[:, None]
    present = above_mode[:, None, None, :] & in_reach[None, None, :, :]
    return jnp.where(present, code_draw, -1).astype(jnp.int32)


def touch_ends(values, stream_key, low, top_value):
    longest = values.shape.index(max(values.shape))
    spots = []
    for shift in (0, 1):
        where = [jax.random.randint(jax.random.fold_in(stream_key, axis), (), 0, length) for axis, length in enumerate(values.shape)]
        where[longest] = (where[longest] + shift) % values.shape[longest]
        spots.append(tuple(where))
    return values.at[spots[0]].set(low).at[spots[1]].set(top_value)


def levels(stream_key, shape, pieces, low, high):
    loudness = 1.0
    for axis_at, shards_of in pieces:
        steps = jax.random.uniform(jax.random.fold_in(jax.random.fold_in(stream_key, 6), axis_at), (shards_of,), jnp.float32, low / len(pieces), high / len(pieces))
        loudness = loudness * jnp.repeat(jnp.exp(steps), shape[axis_at] // shards_of).reshape((-1,) + (1,) * (len(shape) - 1 - axis_at))
    return loudness


def bell_draw(key, dims, scale, limit, cuts=(), kind=jnp.bfloat16):
    level = levels(key, dims, cuts, -0.22, 0.18) if cuts else 1.0
    array = jax.random.normal(key, dims, jnp.float32) * scale * level
    return jnp.minimum(jnp.maximum(array, -limit), limit).astype(kind)


def setup_inputs(seed: int = 0) -> dict:
    keys = jax.random.split(jax.random.key(seed), 7)
    visibility = bell_draw(keys[0], (CHANNEL_COUNT, 2, TIME_SAMPLES, BASELINE_COUNT), 1.0, 6.0, ((0, 4), (2, 64)), jnp.float32)
    codebook = bell_draw(keys[1], (MULTIPOLE_BLOCKS, PATTERN_CODES, BLOCK_WIDTH, 2 * BLOCK_WIDTH), BASELINE_COUNT ** -0.5, 0.1875)
    block_index = draw_block_index(jax.random.fold_in(keys[6], 71), 0)
    block_scale = jnp.clip(jnp.exp(math.log(2.0) - 1.3862944 * jax.random.uniform(keys[3], (MODES, CHANNEL_COUNT, BBLOCKS, MULTIPOLE_BLOCKS), jnp.float32) ** levels(keys[3], (MODES, CHANNEL_COUNT, BBLOCKS, MULTIPOLE_BLOCKS), ((0, 64), (1, 4)), -0.2, 0.2)), 0.5, 2.0)
    fg_basis = bell_draw(keys[4], (MULTIPOLE_BLOCKS, CHANNEL_COUNT, CHANNEL_COUNT), CHANNEL_COUNT ** -0.5, 0.75, (), jnp.float32)
    fg_count = touch_ends(jax.random.randint(keys[5], (MODES,), 1, CHANNEL_COUNT // 2 + 1), jax.random.fold_in(keys[5], 1), 1, (CHANNEL_COUNT // 2 + 1) - 1).astype(jnp.int32)
    return {"visibility": visibility, "codebook": codebook, "block_index": block_index, "block_scale": block_scale, "fg_basis": fg_basis, "fg_count": fg_count}


def realify(codebook):
    half = codebook.shape[-1] // 2
    real_part = codebook[..., :half]
    imag_part = codebook[..., half:]
    upper = jnp.concatenate([real_part, -imag_part], axis=-1)
    lower = jnp.concatenate([imag_part, real_part], axis=-1)
    return jnp.concatenate([upper, lower], axis=-2)


def reference(visibility, codebook, block_index, block_scale, fg_basis, fg_count):
    selected = (MSTEP * jnp.arange(MODES, dtype=jnp.int32)).astype(jnp.int32)
    norm_factor = float(TIME_SAMPLES) ** -0.5

    def transform(channel):
        spectrum_re = jnp.fft.rfft(channel[0], axis=0)[selected]
        spectrum_im = jnp.fft.rfft(channel[1], axis=0)[selected]
        real_part = jnp.real(spectrum_re) - jnp.imag(spectrum_im)
        imag_part = jnp.imag(spectrum_re) + jnp.real(spectrum_im)
        return jnp.stack([real_part, imag_part], axis=1) * norm_factor

    spectra = lax.map(transform, visibility)
    spectra = jnp.transpose(spectra, (1, 0, 2, 3)).astype(jnp.bfloat16)
    code_matrix = realify(codebook).astype(jnp.float32)
    pattern_ids = jnp.arange(PATTERN_CODES, dtype=jnp.int32)
    mode_ids = jnp.arange(CHANNEL_COUNT, dtype=jnp.int32)

    def project(items):
        spectrum, index_rows, scale_rows, count = items
        vectors = spectrum.reshape(CHANNEL_COUNT, 2, BBLOCKS, BLOCK_WIDTH)
        vectors = jnp.transpose(vectors, (0, 2, 1, 3)).reshape(CHANNEL_COUNT, BBLOCKS, 2 * BLOCK_WIDTH).astype(jnp.float32)
        block_selector = jnp.where(index_rows[..., None] == pattern_ids, scale_rows[..., None], jnp.float32(0.0))
        combined = jnp.einsum("fblp,fbi->flpi", block_selector, vectors, precision=lax.Precision.HIGHEST)
        projected = jnp.einsum("flpi,lpij->flj", combined, code_matrix, precision=lax.Precision.HIGHEST)
        projected = lax.optimization_barrier(projected.astype(jnp.bfloat16)).astype(jnp.float32)
        filtered = jnp.einsum("lfk,flj->klj", fg_basis, projected, precision=lax.Precision.HIGHEST)
        retained = mode_ids >= count
        return jnp.where(retained[:, None, None], filtered, jnp.float32(0.0))

    return lax.map(project, (spectra, block_index, block_scale, fg_count))
```

```python
import math

import jax
import jax.numpy as jnp
import numpy as np
from jax import lax
from jax.sharding import Mesh
from jax.sharding import PartitionSpec as P

ELLS = 1024
TM_AXES = ("ty", "tz", "tc")


def realify(codebook):
    half = codebook.shape[-1] // 2
    real_part = codebook[..., :half]
    imag_part = codebook[..., half:]
    upper = jnp.concatenate([real_part, -imag_part], axis=-1)
    lower = jnp.concatenate([imag_part, real_part], axis=-1)
    return jnp.concatenate([upper, lower], axis=-2)


def phases(mode_values, time_index, sidereal_period):
    product = mode_values[:, None] * time_index[None, :] % sidereal_period
    angle = product.astype(jnp.float32) * jnp.float32(2.0 * math.pi / sidereal_period)
    return (jnp.cos(angle), jnp.sin(angle))


def apply_dft(cosine_table, sine_table, samples, norm_factor):
    with_cos = jnp.einsum("mt,fctb->mfcb", cosine_table, samples, precision=lax.Precision.HIGHEST)
    with_sin = jnp.einsum("mt,fctb->mfcb", sine_table, samples, precision=lax.Precision.HIGHEST)
    real_part = with_cos[:, :, 0] + with_sin[:, :, 1]
    imag_part = with_cos[:, :, 1] - with_sin[:, :, 0]
    return jnp.stack([real_part, imag_part], axis=2) * norm_factor


def ring_reduce_scatter(x, axis, n):
    i = lax.axis_index(axis)
    h = x.shape[1] // 2
    xa, xb = x[:, :h], x[:, h:]
    fwd = [(j, (j + 1) % n) for j in range(n)]
    bwd = [(j, (j - 1) % n) for j in range(n)]

    def take(a, k):
        return lax.dynamic_index_in_dim(a, k % n, 0, keepdims=False)

    sa = take(xa, i - 1)
    sb = take(xb, i + 1)
    for k in range(n - 1):
        sa = lax.ppermute(sa, axis, fwd) + take(xa, i - k - 2)
        sb = lax.ppermute(sb, axis, bwd) + take(xb, i + k + 2)
    return jnp.concatenate([sa, sb], axis=0)


def time_reduce_scatter(x, ny, nz):
    c = lax.axis_index("tc")
    y = x.reshape(ny * nz, 2, *x.shape[1:])
    mine = lax.dynamic_index_in_dim(y, c, 1, keepdims=False)
    other = lax.dynamic_index_in_dim(y, 1 - c, 1, keepdims=False)
    y = mine + lax.ppermute(other, "tc", [(0, 1), (1, 0)])
    y = y.reshape(ny, nz, *x.shape[1:])
    h = y.shape[2] // 2
    a = jnp.moveaxis(y[:, :, :h], 1, 0)
    a = ring_reduce_scatter(ring_reduce_scatter(a, "tz", nz), "ty", ny)
    b = ring_reduce_scatter(ring_reduce_scatter(y[:, :, h:], "ty", ny), "tz", nz)
    return jnp.concatenate([a, b], axis=0)[None]


def local(visibility, codebook, block_index, block_scale, fg_basis, fg_count, ny, nz):
    tm_count = ny * nz * 2
    fr_count = lax.axis_size("freq")
    chans_dev = visibility.shape[0]
    time_dev = visibility.shape[2]
    base_all = visibility.shape[3]
    modes_dev = block_index.shape[0]
    modes_all = modes_dev * tm_count
    mode_step = 2 * (ELLS // (2 * modes_all)) - 1
    code_count = codebook.shape[1]
    block_len = codebook.shape[2]
    bblocks = base_all // block_len
    sidereal_period = time_dev * tm_count
    norm_factor = float(sidereal_period) ** (-0.5)
    tm_pos = (lax.axis_index("ty") * nz + lax.axis_index("tz")) * 2 + lax.axis_index("tc")
    time_index = tm_pos * time_dev + jnp.arange(time_dev, dtype=jnp.int32)
    mode_values = mode_step * jnp.arange(modes_all, dtype=jnp.int32)
    cosine_table, sine_table = phases(mode_values, time_index, sidereal_period)
    partial = apply_dft(cosine_table, sine_table, visibility, norm_factor)
    spectra = time_reduce_scatter(partial, ny, nz).astype(jnp.bfloat16)
    vectors = spectra.reshape(modes_dev, chans_dev, 2, bblocks, block_len)
    vectors = jnp.transpose(vectors, (0, 1, 3, 2, 4)).reshape(
        modes_dev, chans_dev, bblocks, 2 * block_len
    )
    vectors = vectors.astype(jnp.float32)
    code_matrix = realify(codebook).astype(jnp.float32)
    block_selector = jnp.where(
        block_index[..., None] == jnp.arange(code_count, dtype=jnp.int32),
        block_scale[..., None],
        jnp.float32(0.0),
    )
    combined = jnp.einsum(
        "mfblp,mfbi->mflpi", block_selector, vectors, precision=lax.Precision.HIGHEST
    )
    weights = jnp.einsum("mflpi,lpij->mflj", combined, code_matrix, precision=lax.Precision.HIGHEST)
    weights_bf = weights.astype(jnp.bfloat16)
    fr_pos = lax.axis_index("freq")
    basis_cols = lax.dynamic_slice_in_dim(fg_basis, fr_pos * chans_dev, chans_dev, 2)
    basis_cols = basis_cols.reshape(fg_basis.shape[0], fr_count, chans_dev, chans_dev)
    summed = None
    for s in range(fr_count):
        if s == 0:
            got = weights_bf
        else:
            got = lax.ppermute(weights_bf, "freq", [(j, (j + s) % fr_count) for j in range(fr_count)])
        rows = lax.dynamic_index_in_dim(basis_cols, (fr_pos - s) % fr_count, 1, keepdims=False)
        term = jnp.einsum(
            "lfk,mflj->mklj", rows, got.astype(jnp.float32), precision=lax.Precision.HIGHEST
        )
        summed = term if summed is None else summed + term
    mode_index = fr_pos * chans_dev + jnp.arange(chans_dev, dtype=jnp.int32)
    retained = mode_index[None, :] >= fg_count[:, None]
    return jnp.where(retained[:, :, None, None], summed, jnp.float32(0.0))


def solution(mesh):
    tm_count = mesh.shape["tm"]
    nz = 8 if tm_count % 16 == 0 else 1
    ny = tm_count // (2 * nz)
    devices = np.asarray(mesh.devices).reshape(ny, nz, 2, mesh.shape["freq"])
    split_mesh = Mesh(devices, TM_AXES + ("freq",))
    placed = (
        P("freq", None, TM_AXES, None),
        P(),
        P(TM_AXES, "freq", None, None),
        P(TM_AXES, "freq", None, None),
        P(),
        P(TM_AXES),
    )

    def body(*args):
        return local(*args, ny=ny, nz=nz)

    return jax.shard_map(
        body, mesh=split_mesh, in_specs=placed, out_specs=P(TM_AXES, "freq", None, None), check_vma=False
    )
```

```python
import math

import jax
import jax.numpy as jnp
import numpy as np
from jax import lax
from jax.sharding import Mesh
from jax.sharding import PartitionSpec as P

ELLS = 1024
TM_AXES = ("ty", "tz", "tc")


def realify(codebook):
    half = codebook.shape[-1] // 2
    real_part = codebook[..., :half]
    imag_part = codebook[..., half:]
    upper = jnp.concatenate([real_part, -imag_part], axis=-1)
    lower = jnp.concatenate([imag_part, real_part], axis=-1)
    return jnp.concatenate([upper, lower], axis=-2)


def phases(mode_values, time_index, sidereal_period):
    product = mode_values[:, None] * time_index[None, :] % sidereal_period
    angle = product.astype(jnp.float32) * jnp.float32(2.0 * math.pi / sidereal_period)
    return (jnp.cos(angle), jnp.sin(angle))


def ring_reduce_scatter(x, axis, n):
    i = lax.axis_index(axis)
    h = x.shape[1] // 2
    xa, xb = x[:, :h], x[:, h:]
    fwd = [(j, (j + 1) % n) for j in range(n)]
    bwd = [(j, (j - 1) % n) for j in range(n)]

    def take(a, k):
        return lax.dynamic_index_in_dim(a, k % n, 0, keepdims=False)

    sa = take(xa, i - 1)
    sb = take(xb, i + 1)
    for k in range(n - 1):
        sa = lax.ppermute(sa, axis, fwd) + take(xa, i - k - 2)
        sb = lax.ppermute(sb, axis, bwd) + take(xb, i + k + 2)
    return jnp.concatenate([sa, sb], axis=0)


def dft_table(mode_values, time_index, sidereal_period, norm_factor):
    cosine, sine = phases(mode_values, time_index, sidereal_period)
    cosine = cosine * jnp.float32(norm_factor)
    sine = sine * jnp.float32(norm_factor)
    return jnp.stack([jnp.stack([cosine, sine], 1), jnp.stack([-sine, cosine], 1)], 1)


def spectra_of(visibility, time_index, sidereal_period, norm_factor, mode_step, ny, nz):
    c = lax.axis_index("tc")
    h = visibility.shape[0] // 2
    jy = jnp.arange(ny, dtype=jnp.int32)
    jz = jnp.arange(nz, dtype=jnp.int32)
    halves = []
    for part, z_major in ((visibility[:h], True), (visibility[h:], False)):
        if z_major:
            pair = (jy[None, :] * nz + jz[:, None]).reshape(-1)
        else:
            pair = (jy[:, None] * nz + jz[None, :]).reshape(-1)
        rows = jnp.concatenate([pair * 2 + (1 - c), pair * 2 + c])
        table = dft_table(mode_step * rows, time_index, sidereal_period, norm_factor)
        out = jnp.einsum("rdct,fctb->rdfb", table, part, precision=lax.Precision.HIGH)
        half_rows = ny * nz
        y = out[half_rows:] + lax.ppermute(out[:half_rows], "tc", [(0, 1), (1, 0)])
        if z_major:
            y = y.reshape(nz, ny, *y.shape[1:])
            y = ring_reduce_scatter(ring_reduce_scatter(y, "tz", nz), "ty", ny)
        else:
            y = y.reshape(ny, nz, *y.shape[1:])
            y = ring_reduce_scatter(ring_reduce_scatter(y, "ty", ny), "tz", nz)
        halves.append(y)
    return jnp.concatenate(halves, axis=1)


def local(visibility, codebook, block_index, block_scale, fg_basis, fg_count, ny, nz):
    tm_count = ny * nz * 2
    fr_count = lax.axis_size("freq")
    chans_dev = visibility.shape[0]
    time_dev = visibility.shape[2]
    base_all = visibility.shape[3]
    modes_dev = block_index.shape[0]
    modes_all = modes_dev * tm_count
    mode_step = 2 * (ELLS // (2 * modes_all)) - 1
    code_count = codebook.shape[1]
    block_len = codebook.shape[2]
    bblocks = base_all // block_len
    sidereal_period = time_dev * tm_count
    norm_factor = float(sidereal_period) ** (-0.5)
    tm_pos = (lax.axis_index("ty") * nz + lax.axis_index("tz")) * 2 + lax.axis_index("tc")
    time_index = tm_pos * time_dev + jnp.arange(time_dev, dtype=jnp.int32)
    spectra = spectra_of(visibility, time_index, sidereal_period, norm_factor, mode_step, ny, nz)
    spectra = spectra.astype(jnp.bfloat16)
    vectors = spectra.reshape(modes_dev, 2, chans_dev, bblocks, block_len)
    vectors = jnp.transpose(vectors, (0, 2, 3, 1, 4)).reshape(
        modes_dev, chans_dev, bblocks, 2 * block_len
    )
    vectors = vectors.astype(jnp.float32)
    code_matrix = realify(codebook).astype(jnp.float32)
    block_selector = jnp.where(
        block_index[..., None] == jnp.arange(code_count, dtype=jnp.int32),
        block_scale[..., None],
        jnp.float32(0.0),
    )
    combined = jnp.einsum(
        "mfblp,mfbi->mflpi", block_selector, vectors, precision=lax.Precision.HIGHEST
    )
    weights = jnp.einsum("mflpi,lpij->mflj", combined, code_matrix, precision=lax.Precision.HIGHEST)
    weights_bf = weights.astype(jnp.bfloat16)
    fr_pos = lax.axis_index("freq")
    basis_cols = lax.dynamic_slice_in_dim(fg_basis, fr_pos * chans_dev, chans_dev, 2)
    basis_cols = basis_cols.reshape(fg_basis.shape[0], fr_count, chans_dev, chans_dev)
    summed = None
    for s in range(fr_count):
        if s == 0:
            got = weights_bf
        else:
            got = lax.ppermute(weights_bf, "freq", [(j, (j + s) % fr_count) for j in range(fr_count)])
        rows = lax.dynamic_index_in_dim(basis_cols, (fr_pos - s) % fr_count, 1, keepdims=False)
        term = jnp.einsum(
            "lfk,mflj->mklj", rows, got.astype(jnp.float32), precision=lax.Precision.HIGHEST
        )
        summed = term if summed is None else summed + term
    mode_index = fr_pos * chans_dev + jnp.arange(chans_dev, dtype=jnp.int32)
    retained = mode_index[None, :] >= fg_count[:, None]
    return jnp.where(retained[:, :, None, None], summed, jnp.float32(0.0))


def solution(mesh):
    tm_count = mesh.shape["tm"]
    nz = 8 if tm_count % 16 == 0 else 1
    ny = tm_count // (2 * nz)
    devices = np.asarray(mesh.devices).reshape(ny, nz, 2, mesh.shape["freq"])
    split_mesh = Mesh(devices, TM_AXES + ("freq",))
    placed = (
        P("freq", None, TM_AXES, None),
        P(),
        P(TM_AXES, "freq", None, None),
        P(TM_AXES, "freq", None, None),
        P(),
        P(TM_AXES),
    )

    def body(*args):
        return local(*args, ny=ny, nz=nz)

    return jax.shard_map(
        body, mesh=split_mesh, in_specs=placed, out_specs=P(TM_AXES, "freq", None, None), check_vma=False
    )
```

```python
import math

import jax
import jax.numpy as jnp
import numpy as np
from jax import lax
from jax.sharding import Mesh
from jax.sharding import PartitionSpec as P

ELLS = 1024
TM_AXES = ("ty", "tz", "tc")


def realify(codebook):
    half = codebook.shape[-1] // 2
    real_part = codebook[..., :half]
    imag_part = codebook[..., half:]
    upper = jnp.concatenate([real_part, -imag_part], axis=-1)
    lower = jnp.concatenate([imag_part, real_part], axis=-1)
    return jnp.concatenate([upper, lower], axis=-2)


def phases(mode_values, time_index, sidereal_period):
    product = mode_values[:, None] * time_index[None, :] % sidereal_period
    angle = product.astype(jnp.float32) * jnp.float32(2.0 * math.pi / sidereal_period)
    return (jnp.cos(angle), jnp.sin(angle))


def dft_table(mode_values, time_index, sidereal_period, norm_factor):
    cosine, sine = phases(mode_values, time_index, sidereal_period)
    cosine = cosine * jnp.float32(norm_factor)
    sine = sine * jnp.float32(norm_factor)
    return jnp.stack([jnp.stack([cosine, sine], 1), jnp.stack([-sine, cosine], 1)], 1)


def spectra_of(visibility, time_index, sidereal_period, norm_factor, mode_step, ny, nz):
    c = lax.axis_index("tc")
    h = visibility.shape[0] // 2
    jy = jnp.arange(ny, dtype=jnp.int32)
    jz = jnp.arange(nz, dtype=jnp.int32)
    chains = []
    for part, z_major in ((visibility[:h], True), (visibility[h:], False)):
        if z_major:
            pair = (jy[None, :] * nz + jz[:, None]).reshape(-1)
            phases_of = (("tz", nz), ("ty", ny))
        else:
            pair = (jy[:, None] * nz + jz[None, :]).reshape(-1)
            phases_of = (("ty", ny), ("tz", nz))
        rows = jnp.concatenate([pair * 2 + (1 - c), pair * 2 + c])
        table = dft_table(mode_step * rows, time_index, sidereal_period, norm_factor)
        out = jnp.einsum("rdct,fctb->rdfb", table, part, precision=lax.Precision.HIGH)
        half_rows = ny * nz
        y = out[half_rows:] + lax.ppermute(out[:half_rows], "tc", [(0, 1), (1, 0)])
        y = y.reshape(phases_of[0][1], phases_of[1][1], *y.shape[1:])
        chains.append({"x": y, "phases": list(phases_of)})
    for ch in chains:
        ch["steps"] = [(ax, n, k) for ax, n in ch["phases"] for k in range(n - 1)]
    rounds = max(len(ch["steps"]) for ch in chains)

    def take(a, k, n):
        return lax.dynamic_index_in_dim(a, k % n, 0, keepdims=False)

    def begin(ch, ax, n):
        i = lax.axis_index(ax)
        x = ch["x"]
        hh = x.shape[1] // 2
        ch["xa"], ch["xb"] = x[:, :hh], x[:, hh:]
        ch["sa"] = take(ch["xa"], i - 1, n)
        ch["sb"] = take(ch["xb"], i + 1, n)

    for ch in chains:
        begin(ch, *ch["steps"][0][:2])
    for r in range(rounds):
        live = [ch for ch in chains if r < len(ch["steps"])]
        sends = lax.optimization_barrier(tuple(v for ch in live for v in (ch["sa"], ch["sb"])))
        for idx, ch in enumerate(live):
            ax, n, k = ch["steps"][r]
            i = lax.axis_index(ax)
            fwd = [(j, (j + 1) % n) for j in range(n)]
            bwd = [(j, (j - 1) % n) for j in range(n)]
            ch["sa"] = lax.ppermute(sends[2 * idx], ax, fwd) + take(ch["xa"], i - k - 2, n)
            ch["sb"] = lax.ppermute(sends[2 * idx + 1], ax, bwd) + take(ch["xb"], i + k + 2, n)
            if k == n - 2:
                ch["x"] = jnp.concatenate([ch["sa"], ch["sb"]], axis=0)
                if r + 1 < len(ch["steps"]):
                    begin(ch, *ch["steps"][r + 1][:2])
    return jnp.concatenate([ch["x"] for ch in chains], axis=1)


def local(visibility, codebook, block_index, block_scale, fg_basis, fg_count, ny, nz):
    tm_count = ny * nz * 2
    fr_count = lax.axis_size("freq")
    chans_dev = visibility.shape[0]
    time_dev = visibility.shape[2]
    base_all = visibility.shape[3]
    modes_dev = block_index.shape[0]
    modes_all = modes_dev * tm_count
    mode_step = 2 * (ELLS // (2 * modes_all)) - 1
    code_count = codebook.shape[1]
    block_len = codebook.shape[2]
    bblocks = base_all // block_len
    sidereal_period = time_dev * tm_count
    norm_factor = float(sidereal_period) ** (-0.5)
    tm_pos = (lax.axis_index("ty") * nz + lax.axis_index("tz")) * 2 + lax.axis_index("tc")
    time_index = tm_pos * time_dev + jnp.arange(time_dev, dtype=jnp.int32)
    spectra = spectra_of(visibility, time_index, sidereal_period, norm_factor, mode_step, ny, nz)
    spectra = spectra.astype(jnp.bfloat16)
    vectors = spectra.reshape(modes_dev, 2, chans_dev, bblocks, block_len)
    vectors = jnp.transpose(vectors, (0, 2, 3, 1, 4)).reshape(
        modes_dev, chans_dev, bblocks, 2 * block_len
    )
    vectors = vectors.astype(jnp.float32)
    code_matrix = realify(codebook).astype(jnp.float32)
    block_selector = jnp.where(
        block_index[..., None] == jnp.arange(code_count, dtype=jnp.int32),
        block_scale[..., None],
        jnp.float32(0.0),
    )
    combined = jnp.einsum(
        "mfblp,mfbi->mflpi", block_selector, vectors, precision=lax.Precision.HIGHEST
    )
    weights = jnp.einsum("mflpi,lpij->mflj", combined, code_matrix, precision=lax.Precision.HIGHEST)
    weights_bf = weights.astype(jnp.bfloat16)
    fr_pos = lax.axis_index("freq")
    basis_cols = lax.dynamic_slice_in_dim(fg_basis, fr_pos * chans_dev, chans_dev, 2)
    basis_cols = basis_cols.reshape(fg_basis.shape[0], fr_count, chans_dev, chans_dev)
    summed = None
    for s in range(fr_count):
        if s == 0:
            got = weights_bf
        else:
            got = lax.ppermute(weights_bf, "freq", [(j, (j + s) % fr_count) for j in range(fr_count)])
        rows = lax.dynamic_index_in_dim(basis_cols, (fr_pos - s) % fr_count, 1, keepdims=False)
        term = jnp.einsum(
            "lfk,mflj->mklj", rows, got.astype(jnp.float32), precision=lax.Precision.HIGHEST
        )
        summed = term if summed is None else summed + term
    mode_index = fr_pos * chans_dev + jnp.arange(chans_dev, dtype=jnp.int32)
    retained = mode_index[None, :] >= fg_count[:, None]
    return jnp.where(retained[:, :, None, None], summed, jnp.float32(0.0))


def solution(mesh):
    tm_count = mesh.shape["tm"]
    nz = 8 if tm_count % 16 == 0 else 1
    ny = tm_count // (2 * nz)
    devices = np.asarray(mesh.devices).reshape(ny, nz, 2, mesh.shape["freq"])
    split_mesh = Mesh(devices, TM_AXES + ("freq",))
    placed = (
        P("freq", None, TM_AXES, None),
        P(),
        P(TM_AXES, "freq", None, None),
        P(TM_AXES, "freq", None, None),
        P(),
        P(TM_AXES),
    )

    def body(*args):
        return local(*args, ny=ny, nz=nz)

    return jax.shard_map(
        body, mesh=split_mesh, in_specs=placed, out_specs=P(TM_AXES, "freq", None, None), check_vma=False
    )
```

```python
import math

import jax
import jax.numpy as jnp
import numpy as np
from jax import lax
from jax.sharding import Mesh
from jax.sharding import PartitionSpec as P

ELLS = 1024
TM_AXES = ("ty", "tz", "tc")


def realify(codebook):
    half = codebook.shape[-1] // 2
    real_part = codebook[..., :half]
    imag_part = codebook[..., half:]
    upper = jnp.concatenate([real_part, -imag_part], axis=-1)
    lower = jnp.concatenate([imag_part, real_part], axis=-1)
    return jnp.concatenate([upper, lower], axis=-2)


def phases(mode_values, time_index, sidereal_period):
    product = mode_values[:, None] * time_index[None, :] % sidereal_period
    angle = product.astype(jnp.float32) * jnp.float32(2.0 * math.pi / sidereal_period)
    return (jnp.cos(angle), jnp.sin(angle))


def ring_reduce_scatter(x, axis, n):
    i = lax.axis_index(axis)
    fwd = [(j, (j + 1) % n) for j in range(n)]

    def take(a, k):
        return lax.dynamic_index_in_dim(a, k % n, 0, keepdims=False)

    s = take(x, i - 1)
    for k in range(n - 1):
        s = lax.ppermute(s, axis, fwd) + take(x, i - k - 2)
    return s


def dft_table(mode_values, time_index, sidereal_period, norm_factor):
    cosine, sine = phases(mode_values, time_index, sidereal_period)
    cosine = cosine * jnp.float32(norm_factor)
    sine = sine * jnp.float32(norm_factor)
    return jnp.stack([jnp.stack([cosine, sine], 1), jnp.stack([-sine, cosine], 1)], 1)


def spectra_of(visibility, time_index, sidereal_period, norm_factor, mode_step, ny, nz):
    c = lax.axis_index("tc")
    h = visibility.shape[0] // 2
    jy = jnp.arange(ny, dtype=jnp.int32)
    jz = jnp.arange(nz, dtype=jnp.int32)
    halves = []
    for part, z_major in ((visibility[:h], True), (visibility[h:], False)):
        if z_major:
            pair = (jy[None, :] * nz + jz[:, None]).reshape(-1)
        else:
            pair = (jy[:, None] * nz + jz[None, :]).reshape(-1)
        rows = jnp.concatenate([pair * 2 + (1 - c), pair * 2 + c])
        table = dft_table(mode_step * rows, time_index, sidereal_period, norm_factor)
        out = jnp.einsum("rdct,fctb->rdfb", table, part, precision=lax.Precision.HIGH)
        half_rows = ny * nz
        y = out[half_rows:] + lax.ppermute(out[:half_rows], "tc", [(0, 1), (1, 0)])
        if z_major:
            y = y.reshape(nz, ny, *y.shape[1:])
            y = ring_reduce_scatter(ring_reduce_scatter(y, "tz", nz), "ty", ny)
        else:
            y = y.reshape(ny, nz, *y.shape[1:])
            y = ring_reduce_scatter(ring_reduce_scatter(y, "ty", ny), "tz", nz)
        halves.append(y)
    return jnp.concatenate(halves, axis=1)


def local(visibility, codebook, block_index, block_scale, fg_basis, fg_count, ny, nz):
    tm_count = ny * nz * 2
    fr_count = lax.axis_size("freq")
    chans_dev = visibility.shape[0]
    time_dev = visibility.shape[2]
    base_all = visibility.shape[3]
    modes_dev = block_index.shape[0]
    modes_all = modes_dev * tm_count
    mode_step = 2 * (ELLS // (2 * modes_all)) - 1
    code_count = codebook.shape[1]
    block_len = codebook.shape[2]
    bblocks = base_all // block_len
    sidereal_period = time_dev * tm_count
    norm_factor = float(sidereal_period) ** (-0.5)
    tm_pos = (lax.axis_index("ty") * nz + lax.axis_index("tz")) * 2 + lax.axis_index("tc")
    time_index = tm_pos * time_dev + jnp.arange(time_dev, dtype=jnp.int32)
    spectra = spectra_of(visibility, time_index, sidereal_period, norm_factor, mode_step, ny, nz)
    spectra = spectra.astype(jnp.bfloat16)
    vectors = spectra.reshape(modes_dev, 2, chans_dev, bblocks, block_len)
    vectors = jnp.transpose(vectors, (0, 2, 3, 1, 4)).reshape(
        modes_dev, chans_dev, bblocks, 2 * block_len
    )
    vectors = vectors.astype(jnp.float32)
    code_matrix = realify(codebook).astype(jnp.float32)
    block_selector = jnp.where(
        block_index[..., None] == jnp.arange(code_count, dtype=jnp.int32),
        block_scale[..., None],
        jnp.float32(0.0),
    )
    combined = jnp.einsum(
        "mfblp,mfbi->mflpi", block_selector, vectors, precision=lax.Precision.HIGHEST
    )
    weights = jnp.einsum("mflpi,lpij->mflj", combined, code_matrix, precision=lax.Precision.HIGHEST)
    weights_bf = weights.astype(jnp.bfloat16)
    fr_pos = lax.axis_index("freq")
    basis_cols = lax.dynamic_slice_in_dim(fg_basis, fr_pos * chans_dev, chans_dev, 2)
    basis_cols = basis_cols.reshape(fg_basis.shape[0], fr_count, chans_dev, chans_dev)
    summed = None
    for s in range(fr_count):
        if s == 0:
            got = weights_bf
        else:
            got = lax.ppermute(weights_bf, "freq", [(j, (j + s) % fr_count) for j in range(fr_count)])
        rows = lax.dynamic_index_in_dim(basis_cols, (fr_pos - s) % fr_count, 1, keepdims=False)
        term = jnp.einsum(
            "lfk,mflj->mklj", rows, got.astype(jnp.float32), precision=lax.Precision.HIGHEST
        )
        summed = term if summed is None else summed + term
    mode_index = fr_pos * chans_dev + jnp.arange(chans_dev, dtype=jnp.int32)
    retained = mode_index[None, :] >= fg_count[:, None]
    return jnp.where(retained[:, :, None, None], summed, jnp.float32(0.0))


def solution(mesh):
    tm_count = mesh.shape["tm"]
    nz = 8 if tm_count % 16 == 0 else 1
    ny = tm_count // (2 * nz)
    devices = np.asarray(mesh.devices).reshape(ny, nz, 2, mesh.shape["freq"])
    split_mesh = Mesh(devices, TM_AXES + ("freq",))
    placed = (
        P("freq", None, TM_AXES, None),
        P(),
        P(TM_AXES, "freq", None, None),
        P(TM_AXES, "freq", None, None),
        P(),
        P(TM_AXES),
    )

    def body(*args):
        return local(*args, ny=ny, nz=nz)

    return jax.shard_map(
        body, mesh=split_mesh, in_specs=placed, out_specs=P(TM_AXES, "freq", None, None), check_vma=False
    )
```

```python
import math

import jax
import jax.numpy as jnp
import numpy as np
from jax import lax
from jax.sharding import Mesh
from jax.sharding import PartitionSpec as P

ELLS = 1024
TM_AXES = ("ty", "tz", "tc")


def realify(codebook):
    half = codebook.shape[-1] // 2
    real_part = codebook[..., :half]
    imag_part = codebook[..., half:]
    upper = jnp.concatenate([real_part, -imag_part], axis=-1)
    lower = jnp.concatenate([imag_part, real_part], axis=-1)
    return jnp.concatenate([upper, lower], axis=-2)


def phases(mode_values, time_index, sidereal_period):
    product = mode_values[:, None] * time_index[None, :] % sidereal_period
    angle = product.astype(jnp.float32) * jnp.float32(2.0 * math.pi / sidereal_period)
    return (jnp.cos(angle), jnp.sin(angle))


def ring_reduce_scatter(x, axis, n):
    i = lax.axis_index(axis)
    fwd = [(j, (j + 1) % n) for j in range(n)]

    def take(a, k):
        return lax.dynamic_index_in_dim(a, k % n, 0, keepdims=False)

    s = take(x, i - 1)
    for k in range(n - 1):
        got = lax.ppermute(s.astype(jnp.bfloat16), axis, fwd)
        s = got.astype(jnp.float32) + take(x, i - k - 2)
    return s


def dft_table(mode_values, time_index, sidereal_period, norm_factor):
    cosine, sine = phases(mode_values, time_index, sidereal_period)
    cosine = cosine * jnp.float32(norm_factor)
    sine = sine * jnp.float32(norm_factor)
    return jnp.stack([jnp.stack([cosine, sine], 1), jnp.stack([-sine, cosine], 1)], 1)


def spectra_of(visibility, time_index, sidereal_period, norm_factor, mode_step, ny, nz):
    c = lax.axis_index("tc")
    h = visibility.shape[0] // 2
    jy = jnp.arange(ny, dtype=jnp.int32)
    jz = jnp.arange(nz, dtype=jnp.int32)
    halves = []
    for part, z_major in ((visibility[:h], True), (visibility[h:], False)):
        if z_major:
            pair = (jy[None, :] * nz + jz[:, None]).reshape(-1)
        else:
            pair = (jy[:, None] * nz + jz[None, :]).reshape(-1)
        rows = jnp.concatenate([pair * 2 + (1 - c), pair * 2 + c])
        table = dft_table(mode_step * rows, time_index, sidereal_period, norm_factor)
        out = jnp.einsum("rdct,fctb->rdfb", table, part, precision=lax.Precision.HIGH)
        half_rows = ny * nz
        y = out[half_rows:] + lax.ppermute(out[:half_rows], "tc", [(0, 1), (1, 0)])
        if z_major:
            y = y.reshape(nz, ny, *y.shape[1:])
            y = ring_reduce_scatter(ring_reduce_scatter(y, "tz", nz), "ty", ny)
        else:
            y = y.reshape(ny, nz, *y.shape[1:])
            y = ring_reduce_scatter(ring_reduce_scatter(y, "ty", ny), "tz", nz)
        halves.append(y)
    return jnp.concatenate(halves, axis=1)


def local(visibility, codebook, block_index, block_scale, fg_basis, fg_count, ny, nz):
    tm_count = ny * nz * 2
    fr_count = lax.axis_size("freq")
    chans_dev = visibility.shape[0]
    time_dev = visibility.shape[2]
    base_all = visibility.shape[3]
    modes_dev = block_index.shape[0]
    modes_all = modes_dev * tm_count
    mode_step = 2 * (ELLS // (2 * modes_all)) - 1
    code_count = codebook.shape[1]
    block_len = codebook.shape[2]
    bblocks = base_all // block_len
    sidereal_period = time_dev * tm_count
    norm_factor = float(sidereal_period) ** (-0.5)
    tm_pos = (lax.axis_index("ty") * nz + lax.axis_index("tz")) * 2 + lax.axis_index("tc")
    time_index = tm_pos * time_dev + jnp.arange(time_dev, dtype=jnp.int32)
    spectra = spectra_of(visibility, time_index, sidereal_period, norm_factor, mode_step, ny, nz)
    spectra = spectra.astype(jnp.bfloat16)
    vectors = spectra.reshape(modes_dev, 2, chans_dev, bblocks, block_len)
    vectors = jnp.transpose(vectors, (0, 2, 3, 1, 4)).reshape(
        modes_dev, chans_dev, bblocks, 2 * block_len
    )
    vectors = vectors.astype(jnp.float32)
    code_matrix = realify(codebook).astype(jnp.float32)
    block_selector = jnp.where(
        block_index[..., None] == jnp.arange(code_count, dtype=jnp.int32),
        block_scale[..., None],
        jnp.float32(0.0),
    )
    combined = jnp.einsum(
        "mfblp,mfbi->mflpi", block_selector, vectors, precision=lax.Precision.HIGHEST
    )
    weights = jnp.einsum("mflpi,lpij->mflj", combined, code_matrix, precision=lax.Precision.HIGHEST)
    weights_bf = weights.astype(jnp.bfloat16)
    fr_pos = lax.axis_index("freq")
    basis_cols = lax.dynamic_slice_in_dim(fg_basis, fr_pos * chans_dev, chans_dev, 2)
    basis_cols = basis_cols.reshape(fg_basis.shape[0], fr_count, chans_dev, chans_dev)
    summed = None
    for s in range(fr_count):
        if s == 0:
            got = weights_bf
        else:
            got = lax.ppermute(weights_bf, "freq", [(j, (j + s) % fr_count) for j in range(fr_count)])
        rows = lax.dynamic_index_in_dim(basis_cols, (fr_pos - s) % fr_count, 1, keepdims=False)
        term = jnp.einsum(
            "lfk,mflj->mklj", rows, got.astype(jnp.float32), precision=lax.Precision.HIGHEST
        )
        summed = term if summed is None else summed + term
    mode_index = fr_pos * chans_dev + jnp.arange(chans_dev, dtype=jnp.int32)
    retained = mode_index[None, :] >= fg_count[:, None]
    return jnp.where(retained[:, :, None, None], summed, jnp.float32(0.0))


def solution(mesh):
    tm_count = mesh.shape["tm"]
    nz = 8 if tm_count % 16 == 0 else 1
    ny = tm_count // (2 * nz)
    devices = np.asarray(mesh.devices).reshape(ny, nz, 2, mesh.shape["freq"])
    split_mesh = Mesh(devices, TM_AXES + ("freq",))
    placed = (
        P("freq", None, TM_AXES, None),
        P(),
        P(TM_AXES, "freq", None, None),
        P(TM_AXES, "freq", None, None),
        P(),
        P(TM_AXES),
    )

    def body(*args):
        return local(*args, ny=ny, nz=nz)

    return jax.shard_map(
        body, mesh=split_mesh, in_specs=placed, out_specs=P(TM_AXES, "freq", None, None), check_vma=False
    )
```

```python
import math

import jax
import jax.numpy as jnp
import numpy as np
from jax import lax
from jax.sharding import Mesh
from jax.sharding import PartitionSpec as P

ELLS = 1024
TM_AXES = ("ty", "tz", "tc")


def realify(codebook):
    half = codebook.shape[-1] // 2
    real_part = codebook[..., :half]
    imag_part = codebook[..., half:]
    upper = jnp.concatenate([real_part, -imag_part], axis=-1)
    lower = jnp.concatenate([imag_part, real_part], axis=-1)
    return jnp.concatenate([upper, lower], axis=-2)


def phases(mode_values, time_index, sidereal_period):
    product = mode_values[:, None] * time_index[None, :] % sidereal_period
    angle = product.astype(jnp.float32) * jnp.float32(2.0 * math.pi / sidereal_period)
    return (jnp.cos(angle), jnp.sin(angle))


def ring_reduce_scatter(x, axis, n):
    i = lax.axis_index(axis)
    fwd = [(j, (j + 1) % n) for j in range(n)]

    def take(a, k):
        return lax.dynamic_index_in_dim(a, k % n, 0, keepdims=False)

    s = take(x, i - 1)
    for k in range(n - 1):
        got = lax.ppermute(s.astype(jnp.bfloat16), axis, fwd)
        s = got.astype(jnp.float32) + take(x, i - k - 2)
    return s


def dft_table(mode_values, time_index, sidereal_period, norm_factor):
    cosine, sine = phases(mode_values, time_index, sidereal_period)
    cosine = cosine * jnp.float32(norm_factor)
    sine = sine * jnp.float32(norm_factor)
    return jnp.stack([jnp.stack([cosine, sine], 1), jnp.stack([-sine, cosine], 1)], 1)


def spectra_of(visibility, time_index, sidereal_period, norm_factor, mode_step, ny, nz):
    c = lax.axis_index("tc")
    chains = 4 if visibility.shape[0] % 4 == 0 else 2
    h = visibility.shape[0] // chains
    jy = jnp.arange(ny, dtype=jnp.int32)
    jz = jnp.arange(nz, dtype=jnp.int32)
    halves = []
    for q in range(chains):
        part, z_major = visibility[q * h:(q + 1) * h], q % 2 == 0
        if z_major:
            pair = (jy[None, :] * nz + jz[:, None]).reshape(-1)
        else:
            pair = (jy[:, None] * nz + jz[None, :]).reshape(-1)
        rows = jnp.concatenate([pair * 2 + (1 - c), pair * 2 + c])
        table = dft_table(mode_step * rows, time_index, sidereal_period, norm_factor)
        out = jnp.einsum("rdct,fctb->rdfb", table, part, precision=lax.Precision.HIGH)
        half_rows = ny * nz
        y = out[half_rows:] + lax.ppermute(out[:half_rows], "tc", [(0, 1), (1, 0)])
        if z_major:
            y = y.reshape(nz, ny, *y.shape[1:])
            y = ring_reduce_scatter(ring_reduce_scatter(y, "tz", nz), "ty", ny)
        else:
            y = y.reshape(ny, nz, *y.shape[1:])
            y = ring_reduce_scatter(ring_reduce_scatter(y, "ty", ny), "tz", nz)
        halves.append(y)
    return jnp.concatenate(halves, axis=1)


def local(visibility, codebook, block_index, block_scale, fg_basis, fg_count, ny, nz):
    tm_count = ny * nz * 2
    fr_count = lax.axis_size("freq")
    chans_dev = visibility.shape[0]
    time_dev = visibility.shape[2]
    base_all = visibility.shape[3]
    modes_dev = block_index.shape[0]
    modes_all = modes_dev * tm_count
    mode_step = 2 * (ELLS // (2 * modes_all)) - 1
    code_count = codebook.shape[1]
    block_len = codebook.shape[2]
    bblocks = base_all // block_len
    sidereal_period = time_dev * tm_count
    norm_factor = float(sidereal_period) ** (-0.5)
    tm_pos = (lax.axis_index("ty") * nz + lax.axis_index("tz")) * 2 + lax.axis_index("tc")
    time_index = tm_pos * time_dev + jnp.arange(time_dev, dtype=jnp.int32)
    spectra = spectra_of(visibility, time_index, sidereal_period, norm_factor, mode_step, ny, nz)
    spectra = spectra.astype(jnp.bfloat16)
    vectors = spectra.reshape(modes_dev, 2, chans_dev, bblocks, block_len)
    vectors = jnp.transpose(vectors, (0, 2, 3, 1, 4)).reshape(
        modes_dev, chans_dev, bblocks, 2 * block_len
    )
    vectors = vectors.astype(jnp.float32)
    code_matrix = realify(codebook).astype(jnp.float32)
    block_selector = jnp.where(
        block_index[..., None] == jnp.arange(code_count, dtype=jnp.int32),
        block_scale[..., None],
        jnp.float32(0.0),
    )
    combined = jnp.einsum(
        "mfblp,mfbi->mflpi", block_selector, vectors, precision=lax.Precision.HIGH
    )
    weights = jnp.einsum("mflpi,lpij->mflj", combined, code_matrix, precision=lax.Precision.HIGH)
    weights_bf = weights.astype(jnp.bfloat16)
    fr_pos = lax.axis_index("freq")
    basis_cols = lax.dynamic_slice_in_dim(fg_basis, fr_pos * chans_dev, chans_dev, 2)
    basis_cols = basis_cols.reshape(fg_basis.shape[0], fr_count, chans_dev, chans_dev)
    summed = None
    for s in range(fr_count):
        if s == 0:
            got = weights_bf
        else:
            got = lax.ppermute(weights_bf, "freq", [(j, (j + s) % fr_count) for j in range(fr_count)])
        rows = lax.dynamic_index_in_dim(basis_cols, (fr_pos - s) % fr_count, 1, keepdims=False)
        term = jnp.einsum(
            "lfk,mflj->mklj", rows, got.astype(jnp.float32), precision=lax.Precision.HIGHEST
        )
        summed = term if summed is None else summed + term
    mode_index = fr_pos * chans_dev + jnp.arange(chans_dev, dtype=jnp.int32)
    retained = mode_index[None, :] >= fg_count[:, None]
    return jnp.where(retained[:, :, None, None], summed, jnp.float32(0.0))


def solution(mesh):
    tm_count = mesh.shape["tm"]
    nz = 8 if tm_count % 16 == 0 else 1
    ny = tm_count // (2 * nz)
    devices = np.asarray(mesh.devices).reshape(ny, nz, 2, mesh.shape["freq"])
    split_mesh = Mesh(devices, TM_AXES + ("freq",))
    placed = (
        P("freq", None, TM_AXES, None),
        P(),
        P(TM_AXES, "freq", None, None),
        P(TM_AXES, "freq", None, None),
        P(),
        P(TM_AXES),
    )

    def body(*args):
        return local(*args, ny=ny, nz=nz)

    return jax.shard_map(
        body, mesh=split_mesh, in_specs=placed, out_specs=P(TM_AXES, "freq", None, None), check_vma=False
    )
```

```python
import math

import jax
import jax.numpy as jnp
import numpy as np
from jax import lax
from jax.sharding import Mesh
from jax.sharding import PartitionSpec as P

ELLS = 1024
TM_AXES = ("ty", "tz", "tc")


def realify(codebook):
    half = codebook.shape[-1] // 2
    real_part = codebook[..., :half]
    imag_part = codebook[..., half:]
    upper = jnp.concatenate([real_part, -imag_part], axis=-1)
    lower = jnp.concatenate([imag_part, real_part], axis=-1)
    return jnp.concatenate([upper, lower], axis=-2)


def phases(mode_values, time_index, sidereal_period):
    product = mode_values[:, None] * time_index[None, :] % sidereal_period
    angle = product.astype(jnp.float32) * jnp.float32(2.0 * math.pi / sidereal_period)
    return (jnp.cos(angle), jnp.sin(angle))


def ring_reduce_scatter(x, axis, n):
    i = lax.axis_index(axis)
    fwd = [(j, (j + 1) % n) for j in range(n)]

    def take(a, k):
        return lax.dynamic_index_in_dim(a, k % n, 0, keepdims=False)

    s = take(x, i - 1)
    for k in range(n - 1):
        got = lax.ppermute(s.astype(jnp.bfloat16), axis, fwd)
        s = got.astype(jnp.float32) + take(x, i - k - 2)
    return s


def dft_table(mode_values, time_index, sidereal_period, norm_factor):
    cosine, sine = phases(mode_values, time_index, sidereal_period)
    cosine = cosine * jnp.float32(norm_factor)
    sine = sine * jnp.float32(norm_factor)
    return jnp.stack([jnp.stack([cosine, sine], 1), jnp.stack([-sine, cosine], 1)], 1)


def spectra_of(visibility, time_index, sidereal_period, norm_factor, mode_step, ny, nz):
    c = lax.axis_index("tc")
    h = visibility.shape[0] // 2
    jy = jnp.arange(ny, dtype=jnp.int32)
    jz = jnp.arange(nz, dtype=jnp.int32)
    halves = []
    for part, z_major in ((visibility[:h], True), (visibility[h:], False)):
        if z_major:
            pair = (jy[None, :] * nz + jz[:, None]).reshape(-1)
        else:
            pair = (jy[:, None] * nz + jz[None, :]).reshape(-1)
        rows = jnp.concatenate([pair * 2 + (1 - c), pair * 2 + c])
        table = dft_table(mode_step * rows, time_index, sidereal_period, norm_factor)
        out = jnp.einsum("rdct,fctb->rdfb", table, part, precision=lax.Precision.HIGH)
        half_rows = ny * nz
        got = lax.ppermute(out[:half_rows].astype(jnp.bfloat16), "tc", [(0, 1), (1, 0)])
        y = out[half_rows:] + got.astype(jnp.float32)
        if z_major:
            y = y.reshape(nz, ny, *y.shape[1:])
            y = ring_reduce_scatter(ring_reduce_scatter(y, "tz", nz), "ty", ny)
        else:
            y = y.reshape(ny, nz, *y.shape[1:])
            y = ring_reduce_scatter(ring_reduce_scatter(y, "ty", ny), "tz", nz)
        halves.append(y)
    return jnp.concatenate(halves, axis=1)


def local(visibility, codebook, block_index, block_scale, fg_basis, fg_count, ny, nz):
    tm_count = ny * nz * 2
    fr_count = lax.axis_size("freq")
    chans_dev = visibility.shape[0]
    time_dev = visibility.shape[2]
    base_all = visibility.shape[3]
    modes_dev = block_index.shape[0]
    modes_all = modes_dev * tm_count
    mode_step = 2 * (ELLS // (2 * modes_all)) - 1
    code_count = codebook.shape[1]
    block_len = codebook.shape[2]
    bblocks = base_all // block_len
    sidereal_period = time_dev * tm_count
    norm_factor = float(sidereal_period) ** (-0.5)
    tm_pos = (lax.axis_index("ty") * nz + lax.axis_index("tz")) * 2 + lax.axis_index("tc")
    time_index = tm_pos * time_dev + jnp.arange(time_dev, dtype=jnp.int32)
    spectra = spectra_of(visibility, time_index, sidereal_period, norm_factor, mode_step, ny, nz)
    spectra = spectra.astype(jnp.bfloat16)
    vectors = spectra.reshape(modes_dev, 2, chans_dev, bblocks, block_len)
    vectors = jnp.transpose(vectors, (0, 2, 3, 1, 4)).reshape(
        modes_dev, chans_dev, bblocks, 2 * block_len
    )
    vectors = vectors.astype(jnp.float32)
    code_matrix = realify(codebook).astype(jnp.float32)
    block_selector = jnp.where(
        block_index[..., None] == jnp.arange(code_count, dtype=jnp.int32),
        block_scale[..., None],
        jnp.float32(0.0),
    )
    combined = jnp.einsum(
        "mfblp,mfbi->mflpi", block_selector, vectors, precision=lax.Precision.HIGH
    )
    weights = jnp.einsum("mflpi,lpij->mflj", combined, code_matrix, precision=lax.Precision.HIGH)
    weights_bf = weights.astype(jnp.bfloat16)
    fr_pos = lax.axis_index("freq")
    basis_cols = lax.dynamic_slice_in_dim(fg_basis, fr_pos * chans_dev, chans_dev, 2)
    basis_cols = basis_cols.reshape(fg_basis.shape[0], fr_count, chans_dev, chans_dev)
    summed = None
    for s in range(fr_count):
        if s == 0:
            got = weights_bf
        else:
            got = lax.ppermute(weights_bf, "freq", [(j, (j + s) % fr_count) for j in range(fr_count)])
        rows = lax.dynamic_index_in_dim(basis_cols, (fr_pos - s) % fr_count, 1, keepdims=False)
        term = jnp.einsum(
            "lfk,mflj->mklj", rows, got.astype(jnp.float32), precision=lax.Precision.HIGHEST
        )
        summed = term if summed is None else summed + term
    mode_index = fr_pos * chans_dev + jnp.arange(chans_dev, dtype=jnp.int32)
    retained = mode_index[None, :] >= fg_count[:, None]
    return jnp.where(retained[:, :, None, None], summed, jnp.float32(0.0))


def solution(mesh):
    tm_count = mesh.shape["tm"]
    nz = 8 if tm_count % 16 == 0 else 1
    ny = tm_count // (2 * nz)
    devices = np.asarray(mesh.devices).reshape(ny, nz, 2, mesh.shape["freq"])
    split_mesh = Mesh(devices, TM_AXES + ("freq",))
    placed = (
        P("freq", None, TM_AXES, None),
        P(),
        P(TM_AXES, "freq", None, None),
        P(TM_AXES, "freq", None, None),
        P(),
        P(TM_AXES),
    )

    def body(*args):
        return local(*args, ny=ny, nz=nz)

    return jax.shard_map(
        body, mesh=split_mesh, in_specs=placed, out_specs=P(TM_AXES, "freq", None, None), check_vma=False
    )
```

```python
import math

import jax
import jax.numpy as jnp
import numpy as np
from jax import lax
from jax.sharding import Mesh
from jax.sharding import PartitionSpec as P

ELLS = 1024
TM_AXES = ("ty", "tz", "tc")


def realify(codebook):
    half = codebook.shape[-1] // 2
    real_part = codebook[..., :half]
    imag_part = codebook[..., half:]
    upper = jnp.concatenate([real_part, -imag_part], axis=-1)
    lower = jnp.concatenate([imag_part, real_part], axis=-1)
    return jnp.concatenate([upper, lower], axis=-2)


def phases(mode_values, time_index, sidereal_period):
    product = mode_values[:, None] * time_index[None, :] % sidereal_period
    angle = product.astype(jnp.float32) * jnp.float32(2.0 * math.pi / sidereal_period)
    return (jnp.cos(angle), jnp.sin(angle))


def ring_reduce_scatter(x, axis, n):
    i = lax.axis_index(axis)
    fwd = [(j, (j + 1) % n) for j in range(n)]

    def take(a, k):
        return lax.dynamic_index_in_dim(a, k % n, 0, keepdims=False)

    s = take(x, i - 1)
    for k in range(n - 1):
        got = lax.ppermute(s.astype(jnp.bfloat16), axis, fwd)
        s = got.astype(jnp.float32) + take(x, i - k - 2)
    return s


def direct_reduce_scatter(x, axis, n):
    i = lax.axis_index(axis)
    s = lax.dynamic_index_in_dim(x, i, 0, keepdims=False)
    for shift in range(1, n):
        send = lax.dynamic_index_in_dim(x, (i + shift) % n, 0, keepdims=False)
        got = lax.ppermute(send.astype(jnp.bfloat16), axis, [(j, (j + shift) % n) for j in range(n)])
        s = s + got.astype(jnp.float32)
    return s


def dft_table(mode_values, time_index, sidereal_period, norm_factor):
    cosine, sine = phases(mode_values, time_index, sidereal_period)
    cosine = cosine * jnp.float32(norm_factor)
    sine = sine * jnp.float32(norm_factor)
    return jnp.stack([jnp.stack([cosine, sine], 1), jnp.stack([-sine, cosine], 1)], 1)


def spectra_of(visibility, time_index, sidereal_period, norm_factor, mode_step, ny, nz):
    c = lax.axis_index("tc")
    h = visibility.shape[0] // 2
    jy = jnp.arange(ny, dtype=jnp.int32)
    jz = jnp.arange(nz, dtype=jnp.int32)
    halves = []
    for part, z_major in ((visibility[:h], True), (visibility[h:], False)):
        if z_major:
            pair = (jy[None, :] * nz + jz[:, None]).reshape(-1)
        else:
            pair = (jy[:, None] * nz + jz[None, :]).reshape(-1)
        rows = jnp.concatenate([pair * 2 + (1 - c), pair * 2 + c])
        table = dft_table(mode_step * rows, time_index, sidereal_period, norm_factor)
        out = jnp.einsum("rdct,fctb->rdfb", table, part, precision=lax.Precision.HIGH)
        half_rows = ny * nz
        got = lax.ppermute(out[:half_rows].astype(jnp.bfloat16), "tc", [(0, 1), (1, 0)])
        y = out[half_rows:] + got.astype(jnp.float32)
        if z_major:
            y = y.reshape(nz, ny, *y.shape[1:])
            y = direct_reduce_scatter(ring_reduce_scatter(y, "tz", nz), "ty", ny)
        else:
            y = y.reshape(ny, nz, *y.shape[1:])
            y = ring_reduce_scatter(direct_reduce_scatter(y, "ty", ny), "tz", nz)
        halves.append(y)
    return jnp.concatenate(halves, axis=1)


def local(visibility, codebook, block_index, block_scale, fg_basis, fg_count, ny, nz):
    tm_count = ny * nz * 2
    fr_count = lax.axis_size("freq")
    chans_dev = visibility.shape[0]
    time_dev = visibility.shape[2]
    base_all = visibility.shape[3]
    modes_dev = block_index.shape[0]
    modes_all = modes_dev * tm_count
    mode_step = 2 * (ELLS // (2 * modes_all)) - 1
    code_count = codebook.shape[1]
    block_len = codebook.shape[2]
    bblocks = base_all // block_len
    sidereal_period = time_dev * tm_count
    norm_factor = float(sidereal_period) ** (-0.5)
    tm_pos = (lax.axis_index("ty") * nz + lax.axis_index("tz")) * 2 + lax.axis_index("tc")
    time_index = tm_pos * time_dev + jnp.arange(time_dev, dtype=jnp.int32)
    spectra = spectra_of(visibility, time_index, sidereal_period, norm_factor, mode_step, ny, nz)
    spectra = spectra.astype(jnp.bfloat16)
    vectors = spectra.reshape(modes_dev, 2, chans_dev, bblocks, block_len)
    vectors = jnp.transpose(vectors, (0, 2, 3, 1, 4)).reshape(
        modes_dev, chans_dev, bblocks, 2 * block_len
    )
    vectors = vectors.astype(jnp.float32)
    code_matrix = realify(codebook).astype(jnp.float32)
    block_selector = jnp.where(
        block_index[..., None] == jnp.arange(code_count, dtype=jnp.int32),
        block_scale[..., None],
        jnp.float32(0.0),
    )
    combined = jnp.einsum(
        "mfblp,mfbi->mflpi", block_selector, vectors, precision=lax.Precision.HIGH
    )
    weights = jnp.einsum("mflpi,lpij->mflj", combined, code_matrix, precision=lax.Precision.HIGH)
    weights_bf = weights.astype(jnp.bfloat16)
    fr_pos = lax.axis_index("freq")
    basis_cols = lax.dynamic_slice_in_dim(fg_basis, fr_pos * chans_dev, chans_dev, 2)
    basis_cols = basis_cols.reshape(fg_basis.shape[0], fr_count, chans_dev, chans_dev)
    summed = None
    for s in range(fr_count):
        if s == 0:
            got = weights_bf
        else:
            got = lax.ppermute(weights_bf, "freq", [(j, (j + s) % fr_count) for j in range(fr_count)])
        rows = lax.dynamic_index_in_dim(basis_cols, (fr_pos - s) % fr_count, 1, keepdims=False)
        term = jnp.einsum(
            "lfk,mflj->mklj", rows, got.astype(jnp.float32), precision=lax.Precision.HIGHEST
        )
        summed = term if summed is None else summed + term
    mode_index = fr_pos * chans_dev + jnp.arange(chans_dev, dtype=jnp.int32)
    retained = mode_index[None, :] >= fg_count[:, None]
    return jnp.where(retained[:, :, None, None], summed, jnp.float32(0.0))


def solution(mesh):
    tm_count = mesh.shape["tm"]
    nz = 8 if tm_count % 16 == 0 else 1
    ny = tm_count // (2 * nz)
    devices = np.asarray(mesh.devices).reshape(ny, nz, 2, mesh.shape["freq"])
    split_mesh = Mesh(devices, TM_AXES + ("freq",))
    placed = (
        P("freq", None, TM_AXES, None),
        P(),
        P(TM_AXES, "freq", None, None),
        P(TM_AXES, "freq", None, None),
        P(),
        P(TM_AXES),
    )

    def body(*args):
        return local(*args, ny=ny, nz=nz)

    return jax.shard_map(
        body, mesh=split_mesh, in_specs=placed, out_specs=P(TM_AXES, "freq", None, None), check_vma=False
    )
```

```python
import math

import jax
import jax.numpy as jnp
import numpy as np
from jax import lax
from jax.sharding import Mesh
from jax.sharding import PartitionSpec as P

ELLS = 1024
TM_AXES = ("ty", "tz", "tc")


def phases(mode_values, time_index, sidereal_period):
    product = mode_values[:, None] * time_index[None, :] % sidereal_period
    angle = product.astype(jnp.float32) * jnp.float32(2.0 * math.pi / sidereal_period)
    return (jnp.cos(angle), jnp.sin(angle))


def ring_reduce_scatter(x, axis, n):
    i = lax.axis_index(axis)
    fwd = [(j, (j + 1) % n) for j in range(n)]

    def take(a, k):
        return lax.dynamic_index_in_dim(a, k % n, 0, keepdims=False)

    s = take(x, i - 1)
    for k in range(n - 1):
        got = lax.ppermute(s.astype(jnp.bfloat16), axis, fwd)
        s = got.astype(jnp.float32) + take(x, i - k - 2)
    return s


def dft_table(mode_values, time_index, sidereal_period, norm_factor):
    cosine, sine = phases(mode_values, time_index, sidereal_period)
    cosine = cosine * jnp.float32(norm_factor)
    sine = sine * jnp.float32(norm_factor)
    return jnp.stack([jnp.stack([cosine, sine], 1), jnp.stack([-sine, cosine], 1)], 1)


def spectra_of(visibility, time_index, sidereal_period, norm_factor, mode_step, ny, nz):
    c = lax.axis_index("tc")
    h = visibility.shape[0] // 2
    jy = jnp.arange(ny, dtype=jnp.int32)
    jz = jnp.arange(nz, dtype=jnp.int32)
    halves = []
    for part, z_major in ((visibility[:h], True), (visibility[h:], False)):
        if z_major:
            pair = (jy[None, :] * nz + jz[:, None]).reshape(-1)
        else:
            pair = (jy[:, None] * nz + jz[None, :]).reshape(-1)
        rows = jnp.concatenate([pair * 2 + (1 - c), pair * 2 + c])
        table = dft_table(mode_step * rows, time_index, sidereal_period, norm_factor)
        out = jnp.einsum("rdct,fctb->rdfb", table, part, precision=lax.Precision.HIGH)
        half_rows = ny * nz
        got = lax.ppermute(out[:half_rows].astype(jnp.bfloat16), "tc", [(0, 1), (1, 0)])
        y = out[half_rows:] + got.astype(jnp.float32)
        if z_major:
            y = y.reshape(nz, ny, *y.shape[1:])
            y = ring_reduce_scatter(ring_reduce_scatter(y, "tz", nz), "ty", ny)
        else:
            y = y.reshape(ny, nz, *y.shape[1:])
            y = ring_reduce_scatter(ring_reduce_scatter(y, "ty", ny), "tz", nz)
        halves.append(y)
    return jnp.concatenate(halves, axis=1)


def local(visibility, codebook, block_index, block_scale, fg_basis, fg_count, ny, nz):
    tm_count = ny * nz * 2
    fr_count = lax.axis_size("freq")
    chans_dev = visibility.shape[0]
    time_dev = visibility.shape[2]
    base_all = visibility.shape[3]
    modes_dev = block_index.shape[0]
    modes_all = modes_dev * tm_count
    mode_step = 2 * (ELLS // (2 * modes_all)) - 1
    code_count = codebook.shape[1]
    block_len = codebook.shape[2]
    bblocks = base_all // block_len
    sidereal_period = time_dev * tm_count
    norm_factor = float(sidereal_period) ** (-0.5)
    tm_pos = (lax.axis_index("ty") * nz + lax.axis_index("tz")) * 2 + lax.axis_index("tc")
    time_index = tm_pos * time_dev + jnp.arange(time_dev, dtype=jnp.int32)
    spectra = spectra_of(visibility, time_index, sidereal_period, norm_factor, mode_step, ny, nz)
    spectra = spectra.astype(jnp.bfloat16)
    vectors = spectra.reshape(modes_dev, 2, chans_dev, bblocks, block_len)
    vectors = jnp.transpose(vectors, (0, 2, 3, 1, 4)).reshape(
        modes_dev, chans_dev, bblocks, 2 * block_len
    )
    vectors = vectors.astype(jnp.float32)
    block_selector = jnp.where(
        block_index[..., None] == jnp.arange(code_count, dtype=jnp.int32),
        block_scale[..., None],
        jnp.float32(0.0),
    )
    combined = jnp.einsum(
        "mfblp,mfbi->mflpi", block_selector, vectors, precision=lax.Precision.HIGH
    )
    half = block_len
    codes = codebook.astype(jnp.float32)
    from_re = jnp.einsum("mflpi,lpij->mflj", combined[..., :half], codes, precision=lax.Precision.HIGH)
    from_im = jnp.einsum("mflpi,lpij->mflj", combined[..., half:], codes, precision=lax.Precision.HIGH)
    weights = jnp.concatenate(
        [from_re[..., :half] + from_im[..., half:], from_im[..., :half] - from_re[..., half:]], axis=-1
    )
    weights_bf = weights.astype(jnp.bfloat16)
    fr_pos = lax.axis_index("freq")
    basis_cols = lax.dynamic_slice_in_dim(fg_basis, fr_pos * chans_dev, chans_dev, 2)
    basis_cols = basis_cols.reshape(fg_basis.shape[0], fr_count, chans_dev, chans_dev)
    summed = None
    for s in range(fr_count):
        if s == 0:
            got = weights_bf
        else:
            got = lax.ppermute(weights_bf, "freq", [(j, (j + s) % fr_count) for j in range(fr_count)])
        rows = lax.dynamic_index_in_dim(basis_cols, (fr_pos - s) % fr_count, 1, keepdims=False)
        term = jnp.einsum(
            "lfk,mflj->mklj", rows, got.astype(jnp.float32), precision=lax.Precision.HIGHEST
        )
        summed = term if summed is None else summed + term
    mode_index = fr_pos * chans_dev + jnp.arange(chans_dev, dtype=jnp.int32)
    retained = mode_index[None, :] >= fg_count[:, None]
    return jnp.where(retained[:, :, None, None], summed, jnp.float32(0.0))


def solution(mesh):
    tm_count = mesh.shape["tm"]
    nz = 8 if tm_count % 16 == 0 else 1
    ny = tm_count // (2 * nz)
    devices = np.asarray(mesh.devices).reshape(ny, nz, 2, mesh.shape["freq"])
    split_mesh = Mesh(devices, TM_AXES + ("freq",))
    placed = (
        P("freq", None, TM_AXES, None),
        P(),
        P(TM_AXES, "freq", None, None),
        P(TM_AXES, "freq", None, None),
        P(),
        P(TM_AXES),
    )

    def body(*args):
        return local(*args, ny=ny, nz=nz)

    return jax.shard_map(
        body, mesh=split_mesh, in_specs=placed, out_specs=P(TM_AXES, "freq", None, None), check_vma=False
    )
```

```python
import math

import jax
import jax.numpy as jnp
import numpy as np
from jax import lax
from jax.sharding import Mesh
from jax.sharding import PartitionSpec as P

ELLS = 1024
TM_AXES = ("ty", "tz", "tc")


def phases(mode_values, time_index, sidereal_period):
    product = mode_values[:, None] * time_index[None, :] % sidereal_period
    angle = product.astype(jnp.float32) * jnp.float32(2.0 * math.pi / sidereal_period)
    return (jnp.cos(angle), jnp.sin(angle))


def ring_reduce_scatter(x, axis, n):
    i = lax.axis_index(axis)
    fwd = [(j, (j + 1) % n) for j in range(n)]

    def take(a, k):
        return lax.dynamic_index_in_dim(a, k % n, 0, keepdims=False)

    s = take(x, i - 1)
    for k in range(n - 1):
        got = lax.ppermute(s.astype(jnp.bfloat16), axis, fwd)
        s = got.astype(jnp.float32) + take(x, i - k - 2)
    return s


def dft_table(mode_values, time_index, sidereal_period, norm_factor):
    cosine, sine = phases(mode_values, time_index, sidereal_period)
    cosine = cosine * jnp.float32(norm_factor)
    sine = sine * jnp.float32(norm_factor)
    return jnp.stack([jnp.stack([cosine, sine], 1), jnp.stack([-sine, cosine], 1)], 1)


def spectra_of(visibility, time_index, sidereal_period, norm_factor, mode_step, ny, nz):
    c = lax.axis_index("tc")
    h = visibility.shape[0] // 2
    jy = jnp.arange(ny, dtype=jnp.int32)
    jz = jnp.arange(nz, dtype=jnp.int32)
    halves = []
    for part, z_major in ((visibility[:h], True), (visibility[h:], False)):
        if z_major:
            pair = jy[None, :] * nz + jz[:, None]
        else:
            pair = jy[:, None] * nz + jz[None, :]
        n1, n2 = pair.shape

        def block(tc_of):
            rows = (pair * 2 + tc_of).reshape(-1)
            table = dft_table(mode_step * rows, time_index, sidereal_period, norm_factor)
            table = table.reshape(n1, n2, *table.shape[1:])
            return jnp.einsum("uvdct,fctb->uvdfb", table, part, precision=lax.Precision.HIGH)

        got = lax.ppermute(block(1 - c).astype(jnp.bfloat16), "tc", [(0, 1), (1, 0)])
        y = block(c) + got.astype(jnp.float32)
        if z_major:
            y = ring_reduce_scatter(ring_reduce_scatter(y, "tz", nz), "ty", ny)
        else:
            y = ring_reduce_scatter(ring_reduce_scatter(y, "ty", ny), "tz", nz)
        halves.append(y)
    return jnp.concatenate(halves, axis=1)


def local(visibility, codebook, block_index, block_scale, fg_basis, fg_count, ny, nz):
    tm_count = ny * nz * 2
    fr_count = lax.axis_size("freq")
    chans_dev = visibility.shape[0]
    time_dev = visibility.shape[2]
    base_all = visibility.shape[3]
    modes_dev = block_index.shape[0]
    modes_all = modes_dev * tm_count
    mode_step = 2 * (ELLS // (2 * modes_all)) - 1
    code_count = codebook.shape[1]
    block_len = codebook.shape[2]
    bblocks = base_all // block_len
    sidereal_period = time_dev * tm_count
    norm_factor = float(sidereal_period) ** (-0.5)
    tm_pos = (lax.axis_index("ty") * nz + lax.axis_index("tz")) * 2 + lax.axis_index("tc")
    time_index = tm_pos * time_dev + jnp.arange(time_dev, dtype=jnp.int32)
    spectra = spectra_of(visibility, time_index, sidereal_period, norm_factor, mode_step, ny, nz)
    spectra = spectra.astype(jnp.bfloat16)
    vectors = spectra.reshape(modes_dev, 2, chans_dev, bblocks, block_len)
    vectors = jnp.transpose(vectors, (0, 2, 3, 1, 4)).reshape(
        modes_dev, chans_dev, bblocks, 2 * block_len
    )
    vectors = vectors.astype(jnp.float32)
    block_selector = jnp.where(
        block_index[..., None] == jnp.arange(code_count, dtype=jnp.int32),
        block_scale[..., None],
        jnp.float32(0.0),
    )
    combined = jnp.einsum(
        "mfblp,mfbi->mflpi", block_selector, vectors, precision=lax.Precision.HIGH
    )
    half = block_len
    codes = codebook.astype(jnp.float32)
    from_re = jnp.einsum("mflpi,lpij->mflj", combined[..., :half], codes, precision=lax.Precision.HIGH)
    from_im = jnp.einsum("mflpi,lpij->mflj", combined[..., half:], codes, precision=lax.Precision.HIGH)
    weights = jnp.concatenate(
        [from_re[..., :half] + from_im[..., half:], from_im[..., :half] - from_re[..., half:]], axis=-1
    )
    weights_bf = weights.astype(jnp.bfloat16)
    fr_pos = lax.axis_index("freq")
    basis_cols = lax.dynamic_slice_in_dim(fg_basis, fr_pos * chans_dev, chans_dev, 2)
    basis_cols = basis_cols.reshape(fg_basis.shape[0], fr_count, chans_dev, chans_dev)
    summed = None
    for s in range(fr_count):
        if s == 0:
            got = weights_bf
        else:
            got = lax.ppermute(weights_bf, "freq", [(j, (j + s) % fr_count) for j in range(fr_count)])
        rows = lax.dynamic_index_in_dim(basis_cols, (fr_pos - s) % fr_count, 1, keepdims=False)
        term = jnp.einsum(
            "lfk,mflj->mklj", rows, got.astype(jnp.float32), precision=lax.Precision.HIGHEST
        )
        summed = term if summed is None else summed + term
    mode_index = fr_pos * chans_dev + jnp.arange(chans_dev, dtype=jnp.int32)
    retained = mode_index[None, :] >= fg_count[:, None]
    return jnp.where(retained[:, :, None, None], summed, jnp.float32(0.0))


def solution(mesh):
    tm_count = mesh.shape["tm"]
    nz = 8 if tm_count % 16 == 0 else 1
    ny = tm_count // (2 * nz)
    devices = np.asarray(mesh.devices).reshape(ny, nz, 2, mesh.shape["freq"])
    split_mesh = Mesh(devices, TM_AXES + ("freq",))
    placed = (
        P("freq", None, TM_AXES, None),
        P(),
        P(TM_AXES, "freq", None, None),
        P(TM_AXES, "freq", None, None),
        P(),
        P(TM_AXES),
    )

    def body(*args):
        return local(*args, ny=ny, nz=nz)

    return jax.shard_map(
        body, mesh=split_mesh, in_specs=placed, out_specs=P(TM_AXES, "freq", None, None), check_vma=False
    )
```

```python
import math

import jax
import jax.numpy as jnp
import numpy as np
from jax import lax
from jax.sharding import Mesh
from jax.sharding import PartitionSpec as P

ELLS = 1024
TM_AXES = ("ty", "tz", "tc")


def phases(mode_values, time_index, sidereal_period):
    product = mode_values[:, None] * time_index[None, :] % sidereal_period
    angle = product.astype(jnp.float32) * jnp.float32(2.0 * math.pi / sidereal_period)
    return (jnp.cos(angle), jnp.sin(angle))


def ring_reduce_scatter(x, axis, n, first=None):
    i = lax.axis_index(axis)
    fwd = [(j, (j + 1) % n) for j in range(n)]

    def take(a, k):
        return lax.dynamic_index_in_dim(a, k % n, 0, keepdims=False)

    s = take(x, i - 1) if first is None else first
    for k in range(n - 1):
        got = lax.ppermute(s.astype(jnp.bfloat16), axis, fwd)
        s = got.astype(jnp.float32) + take(x, i - k - 2)
    return s


def dft_table(mode_values, time_index, sidereal_period, norm_factor):
    cosine, sine = phases(mode_values, time_index, sidereal_period)
    cosine = cosine * jnp.float32(norm_factor)
    sine = sine * jnp.float32(norm_factor)
    return jnp.stack([jnp.stack([cosine, sine], 1), jnp.stack([-sine, cosine], 1)], 1)


def spectra_of(visibility, time_index, sidereal_period, norm_factor, mode_step, ny, nz):
    c = lax.axis_index("tc")
    h = visibility.shape[0] // 2
    jy = jnp.arange(ny, dtype=jnp.int32)
    jz = jnp.arange(nz, dtype=jnp.int32)
    halves = []
    for part, z_major in ((visibility[:h], True), (visibility[h:], False)):
        if z_major:
            pair = (jy[None, :] * nz + jz[:, None]).reshape(-1)
        else:
            pair = (jy[:, None] * nz + jz[None, :]).reshape(-1)
        rows = jnp.concatenate([pair * 2 + (1 - c), pair * 2 + c])
        table = dft_table(mode_step * rows, time_index, sidereal_period, norm_factor)
        out = jnp.einsum("rdct,fctb->rdfb", table, part, precision=lax.Precision.HIGH)
        half_rows = ny * nz
        ax1, n1, ax2, n2 = ("tz", nz, "ty", ny) if z_major else ("ty", ny, "tz", nz)
        other = out[:half_rows].reshape(n1, n2, *out.shape[1:])
        mine = out[half_rows:].reshape(n1, n2, *out.shape[1:])
        lead = (lax.axis_index(ax1) - 1) % n1
        pair_swap = [(0, 1), (1, 0)]
        head = lax.ppermute(lax.dynamic_index_in_dim(other, lead, 0, keepdims=False).astype(jnp.bfloat16), "tc", pair_swap)
        rest = lax.ppermute(other.astype(jnp.bfloat16), "tc", pair_swap)
        first = lax.dynamic_index_in_dim(mine, lead, 0, keepdims=False) + head.astype(jnp.float32)
        y = mine + rest.astype(jnp.float32)
        y = ring_reduce_scatter(ring_reduce_scatter(y, ax1, n1, first=first), ax2, n2)
        halves.append(y)
    return jnp.concatenate(halves, axis=1)


def local(visibility, codebook, block_index, block_scale, fg_basis, fg_count, ny, nz):
    tm_count = ny * nz * 2
    fr_count = lax.axis_size("freq")
    chans_dev = visibility.shape[0]
    time_dev = visibility.shape[2]
    base_all = visibility.shape[3]
    modes_dev = block_index.shape[0]
    modes_all = modes_dev * tm_count
    mode_step = 2 * (ELLS // (2 * modes_all)) - 1
    code_count = codebook.shape[1]
    block_len = codebook.shape[2]
    bblocks = base_all // block_len
    sidereal_period = time_dev * tm_count
    norm_factor = float(sidereal_period) ** (-0.5)
    tm_pos = (lax.axis_index("ty") * nz + lax.axis_index("tz")) * 2 + lax.axis_index("tc")
    time_index = tm_pos * time_dev + jnp.arange(time_dev, dtype=jnp.int32)
    spectra = spectra_of(visibility, time_index, sidereal_period, norm_factor, mode_step, ny, nz)
    spectra = spectra.astype(jnp.bfloat16)
    vectors = spectra.reshape(modes_dev, 2, chans_dev, bblocks, block_len)
    vectors = jnp.transpose(vectors, (0, 2, 3, 1, 4)).reshape(
        modes_dev, chans_dev, bblocks, 2 * block_len
    )
    vectors = vectors.astype(jnp.float32)
    block_selector = jnp.where(
        block_index[..., None] == jnp.arange(code_count, dtype=jnp.int32),
        block_scale[..., None],
        jnp.float32(0.0),
    )
    combined = jnp.einsum(
        "mfblp,mfbi->mflpi", block_selector, vectors, precision=lax.Precision.HIGH
    )
    half = block_len
    codes = codebook.astype(jnp.float32)
    from_re = jnp.einsum("mflpi,lpij->mflj", combined[..., :half], codes, precision=lax.Precision.HIGH)
    from_im = jnp.einsum("mflpi,lpij->mflj", combined[..., half:], codes, precision=lax.Precision.HIGH)
    weights = jnp.concatenate(
        [from_re[..., :half] + from_im[..., half:], from_im[..., :half] - from_re[..., half:]], axis=-1
    )
    weights_bf = weights.astype(jnp.bfloat16)
    fr_pos = lax.axis_index("freq")
    basis_cols = lax.dynamic_slice_in_dim(fg_basis, fr_pos * chans_dev, chans_dev, 2)
    basis_cols = basis_cols.reshape(fg_basis.shape[0], fr_count, chans_dev, chans_dev)
    summed = None
    for s in range(fr_count):
        if s == 0:
            got = weights_bf
        else:
            got = lax.ppermute(weights_bf, "freq", [(j, (j + s) % fr_count) for j in range(fr_count)])
        rows = lax.dynamic_index_in_dim(basis_cols, (fr_pos - s) % fr_count, 1, keepdims=False)
        term = jnp.einsum(
            "lfk,mflj->mklj", rows, got.astype(jnp.float32), precision=lax.Precision.HIGHEST
        )
        summed = term if summed is None else summed + term
    mode_index = fr_pos * chans_dev + jnp.arange(chans_dev, dtype=jnp.int32)
    retained = mode_index[None, :] >= fg_count[:, None]
    return jnp.where(retained[:, :, None, None], summed, jnp.float32(0.0))


def solution(mesh):
    tm_count = mesh.shape["tm"]
    nz = 8 if tm_count % 16 == 0 else 1
    ny = tm_count // (2 * nz)
    devices = np.asarray(mesh.devices).reshape(ny, nz, 2, mesh.shape["freq"])
    split_mesh = Mesh(devices, TM_AXES + ("freq",))
    placed = (
        P("freq", None, TM_AXES, None),
        P(),
        P(TM_AXES, "freq", None, None),
        P(TM_AXES, "freq", None, None),
        P(),
        P(TM_AXES),
    )

    def body(*args):
        return local(*args, ny=ny, nz=nz)

    return jax.shard_map(
        body, mesh=split_mesh, in_specs=placed, out_specs=P(TM_AXES, "freq", None, None), check_vma=False
    )
```

```python
import math

import jax
import jax.numpy as jnp
import numpy as np
from jax import lax
from jax.sharding import Mesh
from jax.sharding import PartitionSpec as P

ELLS = 1024
TM_AXES = ("ty", "tz", "tc")


def phases(mode_values, time_index, sidereal_period):
    product = mode_values[:, None] * time_index[None, :] % sidereal_period
    angle = product.astype(jnp.float32) * jnp.float32(2.0 * math.pi / sidereal_period)
    return (jnp.cos(angle), jnp.sin(angle))


def ring_reduce_scatter(x, axis, n):
    i = lax.axis_index(axis)
    fwd = [(j, (j + 1) % n) for j in range(n)]

    def take(a, k):
        return lax.dynamic_index_in_dim(a, k % n, 0, keepdims=False)

    s = take(x, i - 1)
    for k in range(n - 1):
        got = lax.ppermute(s.astype(jnp.bfloat16), axis, fwd)
        s = got.astype(jnp.float32) + take(x, i - k - 2)
    return s


def dft_table(mode_values, time_index, sidereal_period, norm_factor):
    cosine, sine = phases(mode_values, time_index, sidereal_period)
    cosine = cosine * jnp.float32(norm_factor)
    sine = sine * jnp.float32(norm_factor)
    return jnp.stack([jnp.stack([cosine, sine], 1), jnp.stack([-sine, cosine], 1)], 1)


def spectra_of(visibility, time_index, sidereal_period, norm_factor, mode_step, ny, nz):
    c = lax.axis_index("tc")
    h = visibility.shape[0] // 2
    jy = jnp.arange(ny, dtype=jnp.int32)
    jz = jnp.arange(nz, dtype=jnp.int32)
    halves = []
    outs = []
    half_rows = ny * nz
    for part, z_major in ((visibility[:h], True), (visibility[h:], False)):
        if z_major:
            pair = (jy[None, :] * nz + jz[:, None]).reshape(-1)
        else:
            pair = (jy[:, None] * nz + jz[None, :]).reshape(-1)
        rows = jnp.concatenate([pair * 2 + (1 - c), pair * 2 + c])
        table = dft_table(mode_step * rows, time_index, sidereal_period, norm_factor)
        outs.append(jnp.einsum("rdct,fctb->rdfb", table, part, precision=lax.Precision.HIGH))
    swapped = lax.ppermute(
        jnp.stack([out[:half_rows] for out in outs]).astype(jnp.bfloat16), "tc", [(0, 1), (1, 0)]
    )
    for q, z_major in ((0, True), (1, False)):
        y = outs[q][half_rows:] + swapped[q].astype(jnp.float32)
        if z_major:
            y = y.reshape(nz, ny, *y.shape[1:])
            y = ring_reduce_scatter(ring_reduce_scatter(y, "tz", nz), "ty", ny)
        else:
            y = y.reshape(ny, nz, *y.shape[1:])
            y = ring_reduce_scatter(ring_reduce_scatter(y, "ty", ny), "tz", nz)
        halves.append(y)
    return jnp.concatenate(halves, axis=1)


def local(visibility, codebook, block_index, block_scale, fg_basis, fg_count, ny, nz):
    tm_count = ny * nz * 2
    fr_count = lax.axis_size("freq")
    chans_dev = visibility.shape[0]
    time_dev = visibility.shape[2]
    base_all = visibility.shape[3]
    modes_dev = block_index.shape[0]
    modes_all = modes_dev * tm_count
    mode_step = 2 * (ELLS // (2 * modes_all)) - 1
    code_count = codebook.shape[1]
    block_len = codebook.shape[2]
    bblocks = base_all // block_len
    sidereal_period = time_dev * tm_count
    norm_factor = float(sidereal_period) ** (-0.5)
    tm_pos = (lax.axis_index("ty") * nz + lax.axis_index("tz")) * 2 + lax.axis_index("tc")
    time_index = tm_pos * time_dev + jnp.arange(time_dev, dtype=jnp.int32)
    spectra = spectra_of(visibility, time_index, sidereal_period, norm_factor, mode_step, ny, nz)
    spectra = spectra.astype(jnp.bfloat16)
    vectors = spectra.reshape(modes_dev, 2, chans_dev, bblocks, block_len)
    vectors = jnp.transpose(vectors, (0, 2, 3, 1, 4)).reshape(
        modes_dev, chans_dev, bblocks, 2 * block_len
    )
    vectors = vectors.astype(jnp.float32)
    block_selector = jnp.where(
        block_index[..., None] == jnp.arange(code_count, dtype=jnp.int32),
        block_scale[..., None],
        jnp.float32(0.0),
    )
    combined = jnp.einsum(
        "mfblp,mfbi->mflpi", block_selector, vectors, precision=lax.Precision.HIGH
    )
    half = block_len
    codes = codebook.astype(jnp.float32)
    from_re = jnp.einsum("mflpi,lpij->mflj", combined[..., :half], codes, precision=lax.Precision.HIGH)
    from_im = jnp.einsum("mflpi,lpij->mflj", combined[..., half:], codes, precision=lax.Precision.HIGH)
    weights = jnp.concatenate(
        [from_re[..., :half] + from_im[..., half:], from_im[..., :half] - from_re[..., half:]], axis=-1
    )
    weights_bf = weights.astype(jnp.bfloat16)
    fr_pos = lax.axis_index("freq")
    basis_cols = lax.dynamic_slice_in_dim(fg_basis, fr_pos * chans_dev, chans_dev, 2)
    basis_cols = basis_cols.reshape(fg_basis.shape[0], fr_count, chans_dev, chans_dev)
    summed = None
    for s in range(fr_count):
        if s == 0:
            got = weights_bf
        else:
            got = lax.ppermute(weights_bf, "freq", [(j, (j + s) % fr_count) for j in range(fr_count)])
        rows = lax.dynamic_index_in_dim(basis_cols, (fr_pos - s) % fr_count, 1, keepdims=False)
        term = jnp.einsum(
            "lfk,mflj->mklj", rows, got.astype(jnp.float32), precision=lax.Precision.HIGHEST
        )
        summed = term if summed is None else summed + term
    mode_index = fr_pos * chans_dev + jnp.arange(chans_dev, dtype=jnp.int32)
    retained = mode_index[None, :] >= fg_count[:, None]
    return jnp.where(retained[:, :, None, None], summed, jnp.float32(0.0))


def solution(mesh):
    tm_count = mesh.shape["tm"]
    nz = 8 if tm_count % 16 == 0 else 1
    ny = tm_count // (2 * nz)
    devices = np.asarray(mesh.devices).reshape(ny, nz, 2, mesh.shape["freq"])
    split_mesh = Mesh(devices, TM_AXES + ("freq",))
    placed = (
        P("freq", None, TM_AXES, None),
        P(),
        P(TM_AXES, "freq", None, None),
        P(TM_AXES, "freq", None, None),
        P(),
        P(TM_AXES),
    )

    def body(*args):
        return local(*args, ny=ny, nz=nz)

    return jax.shard_map(
        body, mesh=split_mesh, in_specs=placed, out_specs=P(TM_AXES, "freq", None, None), check_vma=False
    )
```

```python
import math

import jax
import jax.numpy as jnp
import numpy as np
from jax import lax
from jax.sharding import Mesh
from jax.sharding import PartitionSpec as P

ELLS = 1024
TM_AXES = ("ty", "tz", "tc")


def phases(mode_values, time_index, sidereal_period):
    product = mode_values[:, None] * time_index[None, :] % sidereal_period
    angle = product.astype(jnp.float32) * jnp.float32(2.0 * math.pi / sidereal_period)
    return (jnp.cos(angle), jnp.sin(angle))


def ring_reduce_scatter(x, axis, n):
    i = lax.axis_index(axis)
    fwd = [(j, (j + 1) % n) for j in range(n)]

    m = x.shape[0] // n

    def take(a, k):
        if m == 1:
            return lax.dynamic_index_in_dim(a, k % n, 0, keepdims=False)
        return lax.dynamic_slice_in_dim(a, (k % n) * m, m, 0)

    s = take(x, i - 1)
    for k in range(n - 1):
        got = lax.ppermute(s.astype(jnp.bfloat16), axis, fwd)
        s = got.astype(jnp.float32) + take(x, i - k - 2)
    return s


def dft_table(mode_values, time_index, sidereal_period, norm_factor):
    cosine, sine = phases(mode_values, time_index, sidereal_period)
    cosine = cosine * jnp.float32(norm_factor)
    sine = sine * jnp.float32(norm_factor)
    return jnp.stack([jnp.stack([cosine, sine], 1), jnp.stack([-sine, cosine], 1)], 1)


def spectra_of(visibility, time_index, sidereal_period, norm_factor, mode_step, ny, nz):
    c = lax.axis_index("tc")
    h = visibility.shape[0] // 2
    jy = jnp.arange(ny, dtype=jnp.int32)
    jz = jnp.arange(nz, dtype=jnp.int32)
    halves = []
    for part, z_major in ((visibility[:h], True), (visibility[h:], False)):
        if z_major:
            pair = (jy[None, :] * nz + jz[:, None]).reshape(-1)
        else:
            pair = (jy[:, None] * nz + jz[None, :]).reshape(-1)
        rows = jnp.concatenate([pair * 2 + (1 - c), pair * 2 + c])
        table = dft_table(mode_step * rows, time_index, sidereal_period, norm_factor)
        out = jnp.einsum("rdct,fctb->rdfb", table, part, precision=lax.Precision.HIGH)
        half_rows = ny * nz
        got = lax.ppermute(out[:half_rows].astype(jnp.bfloat16), "tc", [(0, 1), (1, 0)])
        y = out[half_rows:] + got.astype(jnp.float32)
        if z_major:
            y = ring_reduce_scatter(ring_reduce_scatter(y, "tz", nz), "ty", ny)
        else:
            y = ring_reduce_scatter(ring_reduce_scatter(y, "ty", ny), "tz", nz)
        halves.append(y)
    return jnp.concatenate(halves, axis=1)


def local(visibility, codebook, block_index, block_scale, fg_basis, fg_count, ny, nz):
    tm_count = ny * nz * 2
    fr_count = lax.axis_size("freq")
    chans_dev = visibility.shape[0]
    time_dev = visibility.shape[2]
    base_all = visibility.shape[3]
    modes_dev = block_index.shape[0]
    modes_all = modes_dev * tm_count
    mode_step = 2 * (ELLS // (2 * modes_all)) - 1
    code_count = codebook.shape[1]
    block_len = codebook.shape[2]
    bblocks = base_all // block_len
    sidereal_period = time_dev * tm_count
    norm_factor = float(sidereal_period) ** (-0.5)
    tm_pos = (lax.axis_index("ty") * nz + lax.axis_index("tz")) * 2 + lax.axis_index("tc")
    time_index = tm_pos * time_dev + jnp.arange(time_dev, dtype=jnp.int32)
    spectra = spectra_of(visibility, time_index, sidereal_period, norm_factor, mode_step, ny, nz)
    spectra = spectra.astype(jnp.bfloat16)
    vectors = spectra.reshape(modes_dev, 2, chans_dev, bblocks, block_len)
    vectors = jnp.transpose(vectors, (0, 2, 3, 1, 4)).reshape(
        modes_dev, chans_dev, bblocks, 2 * block_len
    )
    vectors = vectors.astype(jnp.float32)
    block_selector = jnp.where(
        block_index[..., None] == jnp.arange(code_count, dtype=jnp.int32),
        block_scale[..., None],
        jnp.float32(0.0),
    )
    combined = jnp.einsum(
        "mfblp,mfbi->mflpi", block_selector, vectors, precision=lax.Precision.HIGH
    )
    half = block_len
    codes = codebook.astype(jnp.float32)
    from_re = jnp.einsum("mflpi,lpij->mflj", combined[..., :half], codes, precision=lax.Precision.HIGH)
    from_im = jnp.einsum("mflpi,lpij->mflj", combined[..., half:], codes, precision=lax.Precision.HIGH)
    weights = jnp.concatenate(
        [from_re[..., :half] + from_im[..., half:], from_im[..., :half] - from_re[..., half:]], axis=-1
    )
    weights_bf = weights.astype(jnp.bfloat16)
    fr_pos = lax.axis_index("freq")
    basis_cols = lax.dynamic_slice_in_dim(fg_basis, fr_pos * chans_dev, chans_dev, 2)
    basis_cols = basis_cols.reshape(fg_basis.shape[0], fr_count, chans_dev, chans_dev)
    summed = None
    for s in range(fr_count):
        if s == 0:
            got = weights_bf
        else:
            got = lax.ppermute(weights_bf, "freq", [(j, (j + s) % fr_count) for j in range(fr_count)])
        rows = lax.dynamic_index_in_dim(basis_cols, (fr_pos - s) % fr_count, 1, keepdims=False)
        term = jnp.einsum(
            "lfk,mflj->mklj", rows, got.astype(jnp.float32), precision=lax.Precision.HIGHEST
        )
        summed = term if summed is None else summed + term
    mode_index = fr_pos * chans_dev + jnp.arange(chans_dev, dtype=jnp.int32)
    retained = mode_index[None, :] >= fg_count[:, None]
    return jnp.where(retained[:, :, None, None], summed, jnp.float32(0.0))


def solution(mesh):
    tm_count = mesh.shape["tm"]
    nz = 8 if tm_count % 16 == 0 else 1
    ny = tm_count // (2 * nz)
    devices = np.asarray(mesh.devices).reshape(ny, nz, 2, mesh.shape["freq"])
    split_mesh = Mesh(devices, TM_AXES + ("freq",))
    placed = (
        P("freq", None, TM_AXES, None),
        P(),
        P(TM_AXES, "freq", None, None),
        P(TM_AXES, "freq", None, None),
        P(),
        P(TM_AXES),
    )

    def body(*args):
        return local(*args, ny=ny, nz=nz)

    return jax.shard_map(
        body, mesh=split_mesh, in_specs=placed, out_specs=P(TM_AXES, "freq", None, None), check_vma=False
    )
```
